256 devices in a mesh: dp: 32 (over x, y, core), shard: 8 (over z).
Axes of the slice: x: 4, y: 4, z: 8, core: 2. Of those that a mesh axis runs over, the one named last changes fastest.
Arguments:
- audio: bfloat16 [65536, 512], P(('dp', 'shard')), may hold values from -6 to 6
- cotangent: bfloat16 [65536, 512], P(('dp', 'shard')), may hold values from -6 to 6
- clip_lengths: int32 [256, 8], P(('dp', 'shard')), may hold values from 1 to 128, 256 in all within a row
- conv_weight: bfloat16 [3584, 512], P('shard'), may hold values from -0.09375 to 0.09375
- mix_weight: bfloat16 [512, 512], P('shard'), may hold values from -0.25 to 0.25
- conv_bias: float32 [512], replicated, may hold values from -3 to 3
- alpha_in: float32 [512], replicated, may hold values from 0.5 to 3
- alpha_mid: float32 [512], replicated, may hold values from 0.5 to 3
Outputs:
- in_grad: bfloat16 [65536, 512], P(('dp', 'shard'))
- conv_grad: float32 [3584, 512], P(('dp', 'shard'))
- mix_grad: float32 [512, 512], P(('dp', 'shard'))
- vector_grad: float32 [4, 512], P(None, ('dp', 'shard'))
The draws below stay inside these ranges and needn't reach their ends.
Inputs may be any that keep to these rules, and one draw needn't show every extreme that they name: `clip_lengths`: each device's clip lengths sum to 256; the largest on each device is 128.
All inputs are finite; a program needn't handle non-finite values.
Results may differ from the reference program's by a relative error of at most 0.01.
Values may be sent and summed in bfloat16 or wider, within the bound.
No kernel may reach another device: no remote copies, remote signals or barrier semaphores. Data moves between devices by JAX's collectives and lax.ppermute only.
A program may use at most 64 MiB of HBM per device.

```python
import math
import jax
import jax.numpy as jnp
import numpy as np
from jax import lax

C = 512
TAPS = 7
DILATION_SIZE = 9
FRAMES_DEV = 256
CLIPS = 8
FRAMES = 65536
DEVICES_ALL = 256


def levels(own_key, extent, cuts, low, largest):
    def one(dim, parts):
        draws = jax.random.uniform(jax.random.fold_in(jax.random.fold_in(own_key, 6), dim), (parts,), jnp.float32, low / len(cuts), largest / len(cuts))
        return jnp.repeat(jnp.exp(draws), extent[dim] // parts).reshape((-1,) + (1,) * (len(extent) - dim - 1))

    loudness = one(*cuts[0])
    for cut in cuts[1:]:
        loudness = loudness * one(*cut)
    return loudness


def split_up(count, total, bound, skew):
    weights = [(1 << 20) // math.isqrt(rank ** skew) + 1 for rank in range(2, count + 1)]
    surplus, given = total - bound - (count - 1), [1] * (count - 1)
    while surplus > 0:
        candidates = [i for i in range(count - 1) if given[i] < bound]
        pool, remaining = sum([weights[i] for i in candidates]), surplus
        for i in candidates:
            addition = min(bound - given[i], max(1, remaining * weights[i] // pool), surplus)
            given[i] = given[i] + addition
            surplus = surplus - addition
    return np.array([bound] + given)


def uneven_parts(own_key, count, total, limit, slope):
    if count == 2:
        one = jax.random.randint(own_key, (), max(1, total - limit), min(limit, total - 1) + 1)
        return jnp.stack([one, total - one])
    tallies = jnp.asarray(split_up(count, total, limit, slope), jnp.int32)
    pairs = (count - 1) // 2
    giver, receiver = tallies[1:1 + 2 * pairs:2], tallies[2:2 + 2 * pairs:2]
    margin = jnp.minimum(giver - 1, limit - receiver)
    shifted = jax.random.randint(jax.random.fold_in(own_key, 1), (pairs,), 0, 1 << 20) % (margin + 1)
    tallies = tallies.at[1:1 + 2 * pairs:2].set(giver - shifted).at[2:2 + 2 * pairs:2].set(receiver + shifted)
    return tallies[jax.random.permutation(jax.random.fold_in(own_key, 2), count)]


def gaussian(key, shape, spread, reach, pieces=(), kind=jnp.bfloat16):
    factor_of = levels(key, shape, pieces, -0.22, 0.18) if pieces else 1.0
    drawn = jax.random.normal(key, shape, jnp.float32) * spread * factor_of
    return jnp.minimum(jnp.maximum(drawn, -reach), reach).astype(kind)


def setup_inputs(seed: int = 0) -> dict:
    key_list = jax.random.split(jax.random.key(seed), 9)
    return {
        "audio": gaussian(key_list[0], (FRAMES, C), 1.0, 6.0, ((0, 256),)),
        "cotangent": gaussian(key_list[1], (FRAMES, C), 1.0, 6.0, ((0, 256),)),
        "clip_lengths": jax.vmap(lambda own: uneven_parts(own, CLIPS, FRAMES_DEV, FRAMES_DEV // 2, 2))(jax.random.split(key_list[2], DEVICES_ALL)).reshape((DEVICES_ALL, CLIPS)).astype(jnp.int32),
        "conv_weight": gaussian(key_list[3], (TAPS * C, C), (TAPS * C) ** -0.5, 0.09375, ((0, 8),)),
        "mix_weight": gaussian(key_list[4], (C, C), C ** -0.5, 0.25, ((0, 8),)),
        "conv_bias": gaussian(key_list[5], (C,), 0.5, 3.0, (), jnp.float32),
        "alpha_in": jnp.clip(jnp.exp(jax.random.uniform(key_list[6], (C,), jnp.float32, math.log(0.5), math.log(3.0))), 0.5, 3.0),
        "alpha_mid": jnp.clip(jnp.exp(jax.random.uniform(key_list[7], (C,), jnp.float32, math.log(0.5), math.log(3.0))), 0.5, 3.0),
    }


def shift_rows(block, tap_offset, fill):
    rows = block.shape[0]
    shift_amount = min(abs(tap_offset), rows)
    if shift_amount == 0:
        return block
    edge_padding = jnp.full((shift_amount,) + block.shape[1:], fill, block.dtype)
    if tap_offset > 0:
        return jnp.concatenate([block[shift_amount:], edge_padding], axis=0)
    return jnp.concatenate([edge_padding, block[:rows - shift_amount]], axis=0)


def clip_masks(lengths_row, rows):
    clip_ends = jnp.cumsum(lengths_row.astype(jnp.int32))
    position = jnp.arange(rows, dtype=jnp.int32)
    clip_id = jnp.sum((position[:, None] >= clip_ends[None, :]).astype(jnp.int32), axis=1).astype(jnp.int32)
    result = []
    for kernel_tap_index in range(TAPS):
        tap_offset = (kernel_tap_index - 3) * DILATION_SIZE
        result.append(shift_rows(clip_id, tap_offset, -1) == clip_id)
    return result


def snake_parts(value, alpha):
    sine = jnp.sin(alpha * value)
    double = jnp.sin(2.0 * alpha * value)
    return value + sine * sine / alpha, 1.0 + double, value * double / alpha - sine * sine / (alpha * alpha)


def local_step(audio_block, cot_block, lengths_row, conv_weight, mix_weight, conv_bias, alpha_in, alpha_mid):
    rows = audio_block.shape[0]
    same_clip_flags = clip_masks(lengths_row, rows)
    audio_f = audio_block.astype(jnp.float32)
    act_in, slope_in, dalpha_in = snake_parts(audio_f, alpha_in)
    first = act_in.astype(jnp.bfloat16)
    columns = []
    for kernel_tap_index in range(TAPS):
        tap_offset = (kernel_tap_index - 3) * DILATION_SIZE
        moved = shift_rows(first, tap_offset, 0)
        columns.append(jnp.where(same_clip_flags[kernel_tap_index][:, None], moved, jnp.zeros_like(moved)))
    unfolded = jnp.concatenate(columns, axis=1)
    pre = jnp.dot(unfolded, conv_weight, preferred_element_type=jnp.float32) + conv_bias
    act_mid, slope_mid, dalpha_mid = snake_parts(pre, alpha_mid)
    second = act_mid.astype(jnp.bfloat16)
    mix_term = jnp.dot(second.T, cot_block, preferred_element_type=jnp.float32)
    second_gradient = jnp.dot(cot_block, mix_weight.T, preferred_element_type=jnp.float32)
    d_pre = (second_gradient * slope_mid).astype(jnp.bfloat16)
    convolution_part = jnp.dot(unfolded.T, d_pre, preferred_element_type=jnp.float32)
    d_unf = jnp.dot(d_pre, conv_weight.T, preferred_element_type=jnp.float32).astype(jnp.bfloat16)
    d_first = jnp.zeros((rows, C), jnp.float32)
    for kernel_tap_index in range(TAPS):
        tap_offset = (kernel_tap_index - 3) * DILATION_SIZE
        piece = d_unf[:, kernel_tap_index * C:(kernel_tap_index + 1) * C].astype(jnp.float32)
        piece = jnp.where(same_clip_flags[kernel_tap_index][:, None], piece, jnp.zeros_like(piece))
        d_first = d_first + shift_rows(piece, -tap_offset, 0.0)
    in_grad = (cot_block.astype(jnp.float32) + d_first * slope_in).astype(jnp.bfloat16)
    vectors = jnp.stack([
        jnp.sum(d_pre.astype(jnp.float32), axis=0),
        jnp.sum(cot_block.astype(jnp.float32), axis=0),
        jnp.sum(d_first * dalpha_in, axis=0),
        jnp.sum(second_gradient * dalpha_mid, axis=0)])
    return in_grad, convolution_part, mix_term, vectors


def reference(audio, cotangent, clip_lengths, conv_weight, mix_weight, conv_bias, alpha_in, alpha_mid):
    blocks = clip_lengths.shape[0]
    audio_blocks = audio.reshape(blocks, FRAMES_DEV, C)
    cot_blocks = cotangent.reshape(blocks, FRAMES_DEV, C)

    def advance(carry, inputs):
        in_grad, convolution_part, mix_term, vectors = local_step(inputs[0], inputs[1], inputs[2], conv_weight, mix_weight, conv_bias, alpha_in, alpha_mid)
        return (carry[0] + convolution_part, carry[1] + mix_term, carry[2] + vectors), in_grad

    start = (jnp.zeros((TAPS * C, C), jnp.float32), jnp.zeros((C, C), jnp.float32), jnp.zeros((4, C), jnp.float32))
    totals, in_grads = lax.scan(advance, start, (audio_blocks, cot_blocks, clip_lengths))
    return in_grads.reshape(blocks * FRAMES_DEV, C), totals[0], totals[1], totals[2]
```

```python
import jax
import jax.numpy as jnp
from jax import lax
from jax.sharding import PartitionSpec as P

C = 512
TAPS = 7
DILATION_SIZE = 9


def shift_rows(block, tap_offset, fill):
    rows = block.shape[0]
    shift_amount = min(abs(tap_offset), rows)
    if shift_amount == 0:
        return block
    edge_padding = jnp.full((shift_amount,) + block.shape[1:], fill, block.dtype)
    if tap_offset > 0:
        return jnp.concatenate([block[shift_amount:], edge_padding], axis=0)
    return jnp.concatenate([edge_padding, block[: rows - shift_amount]], axis=0)


def clip_masks(lengths_row, rows):
    clip_ends = jnp.cumsum(lengths_row)
    position = jnp.arange(rows, dtype=jnp.int32)
    clip_id = jnp.sum((position[:, None] >= clip_ends[None, :]).astype(jnp.int32), axis=1)
    result = []
    for kernel_tap_index in range(TAPS):
        tap_offset = (kernel_tap_index - 3) * DILATION_SIZE
        result.append(shift_rows(clip_id, tap_offset, -1) == clip_id)
    return result


def snake_parts(value, alpha):
    sine = jnp.sin(alpha * value)
    double = jnp.sin(2.0 * alpha * value)
    return (
        value + sine * sine / alpha,
        1.0 + double,
        value * double / alpha - sine * sine / (alpha * alpha),
    )


def per_device(
    audio, cotangent, clip_lengths, conv_weight, mix_weight, conv_bias, alpha_in, alpha_mid
):
    rows = audio.shape[0]
    same_clip_flags = clip_masks(clip_lengths[0], rows)
    conv_rows = conv_weight.shape[0]
    mix_rows = mix_weight.shape[0]
    both = jnp.concatenate([conv_weight, mix_weight], axis=0)
    gathered = lax.all_gather(both, "shard", axis=0, tiled=True)
    gathered = gathered.reshape(-1, conv_rows + mix_rows, C)
    conv_full = gathered[:, :conv_rows].reshape(-1, C)
    mix_full = gathered[:, conv_rows:].reshape(-1, C)
    audio_f = audio.astype(jnp.float32)
    act_in, slope_in, dalpha_in = snake_parts(audio_f, alpha_in)
    first = act_in.astype(jnp.bfloat16)
    columns = []
    for kernel_tap_index in range(TAPS):
        tap_offset = (kernel_tap_index - 3) * DILATION_SIZE
        moved = shift_rows(first, tap_offset, 0)
        columns.append(
            jnp.where(same_clip_flags[kernel_tap_index][:, None], moved, jnp.zeros_like(moved))
        )
    unfolded = jnp.concatenate(columns, axis=1)
    product = jnp.dot(
        unfolded,
        conv_full,
        preferred_element_type=jnp.float32,
    )
    pre = product + conv_bias
    act_mid, slope_mid, dalpha_mid = snake_parts(pre, alpha_mid)
    second = act_mid.astype(jnp.bfloat16)
    mix_term = lax.dot_general(
        second, cotangent, (((0,), (0,)), ((), ())), preferred_element_type=jnp.float32
    )
    second_gradient = lax.dot_general(
        cotangent, mix_full, (((1,), (1,)), ((), ())), preferred_element_type=jnp.float32
    )
    d_pre = (second_gradient * slope_mid).astype(jnp.bfloat16)
    convolution_part = lax.dot_general(
        unfolded, d_pre, (((0,), (0,)), ((), ())), preferred_element_type=jnp.float32
    )
    d_unf = lax.dot_general(
        d_pre,
        conv_full,
        (((1,), (1,)), ((), ())),
        preferred_element_type=jnp.float32,
    ).astype(jnp.bfloat16)
    d_first = jnp.zeros((rows, C), jnp.float32)
    for kernel_tap_index in range(TAPS):
        tap_offset = (kernel_tap_index - 3) * DILATION_SIZE
        piece = d_unf[:, kernel_tap_index * C : (kernel_tap_index + 1) * C].astype(jnp.float32)
        piece = jnp.where(same_clip_flags[kernel_tap_index][:, None], piece, jnp.zeros_like(piece))
        d_first = d_first + shift_rows(piece, -tap_offset, 0.0)
    in_grad = (cotangent.astype(jnp.float32) + d_first * slope_in).astype(jnp.bfloat16)
    vectors = jnp.stack(
        [
            jnp.sum(d_pre.astype(jnp.float32), axis=0),
            jnp.sum(cotangent.astype(jnp.float32), axis=0),
            jnp.sum(d_first * dalpha_in, axis=0),
            jnp.sum(second_gradient * dalpha_mid, axis=0),
        ]
    )
    devices = lax.axis_size(("dp", "shard"))
    conv_each = convolution_part.shape[0] // devices
    mix_each = mix_term.shape[0] // devices
    packed = jnp.concatenate(
        [
            convolution_part.reshape(devices, conv_each, C),
            mix_term.reshape(devices, mix_each, C),
        ],
        axis=1,
    ).reshape(-1, C)
    summed = lax.psum_scatter(packed, ("dp", "shard"), scatter_dimension=0, tiled=True)
    conv_grad = summed[:conv_each]
    mix_grad = summed[conv_each:]
    vector_grad = lax.psum_scatter(vectors, ("dp", "shard"), scatter_dimension=1, tiled=True)
    return (in_grad, conv_grad, mix_grad, vector_grad)


def solution(mesh):
    placed = (
        P(("dp", "shard"), None),
        P(("dp", "shard"), None),
        P(("dp", "shard"), None),
        P("shard", None),
        P("shard", None),
        P(),
        P(),
        P(),
    )
    return jax.shard_map(
        per_device,
        mesh=mesh,
        in_specs=placed,
        out_specs=(
            P(("dp", "shard"), None),
            P(("dp", "shard"), None),
            P(("dp", "shard"), None),
            P(None, ("dp", "shard")),
        ),
        check_vma=False,
    )
```

```python
import jax
import jax.numpy as jnp
from jax import lax
from jax.sharding import Mesh, PartitionSpec as P

C = 512
TAPS = 7
DILATION_SIZE = 9
FRAME_AXES = ("x", "y", "c", "z")
SCATTER_ORDER = ("c", "z", "y", "x")


def shift_rows(block, tap_offset, fill):
    rows = block.shape[0]
    shift_amount = min(abs(tap_offset), rows)
    if shift_amount == 0:
        return block
    edge_padding = jnp.full((shift_amount,) + block.shape[1:], fill, block.dtype)
    if tap_offset > 0:
        return jnp.concatenate([block[shift_amount:], edge_padding], axis=0)
    return jnp.concatenate([edge_padding, block[: rows - shift_amount]], axis=0)


def clip_masks(lengths_row, rows):
    clip_ends = jnp.cumsum(lengths_row)
    position = jnp.arange(rows, dtype=jnp.int32)
    clip_id = jnp.sum((position[:, None] >= clip_ends[None, :]).astype(jnp.int32), axis=1)
    result = []
    for kernel_tap_index in range(TAPS):
        tap_offset = (kernel_tap_index - 3) * DILATION_SIZE
        result.append(shift_rows(clip_id, tap_offset, -1) == clip_id)
    return result


def snake_parts(value, alpha):
    sine = jnp.sin(alpha * value)
    double = jnp.sin(2.0 * alpha * value)
    return (
        value + sine * sine / alpha,
        1.0 + double,
        value * double / alpha - sine * sine / (alpha * alpha),
    )


def per_device(
    audio, cotangent, clip_lengths, conv_weight, mix_weight, conv_bias, alpha_in, alpha_mid
):
    rows = audio.shape[0]
    same_clip_flags = clip_masks(clip_lengths[0], rows)
    conv_rows = conv_weight.shape[0]
    mix_rows = mix_weight.shape[0]
    both = jnp.concatenate([conv_weight, mix_weight], axis=0)
    gathered = lax.all_gather(both, "z", axis=0, tiled=True)
    gathered = gathered.reshape(-1, conv_rows + mix_rows, C)
    conv_full = gathered[:, :conv_rows].reshape(-1, C)
    mix_full = gathered[:, conv_rows:].reshape(-1, C)
    audio_f = audio.astype(jnp.float32)
    act_in, slope_in, dalpha_in = snake_parts(audio_f, alpha_in)
    first = act_in.astype(jnp.bfloat16)
    columns = []
    for kernel_tap_index in range(TAPS):
        tap_offset = (kernel_tap_index - 3) * DILATION_SIZE
        moved = shift_rows(first, tap_offset, 0)
        columns.append(
            jnp.where(same_clip_flags[kernel_tap_index][:, None], moved, jnp.zeros_like(moved))
        )
    unfolded = jnp.concatenate(columns, axis=1)
    product = jnp.dot(
        unfolded,
        conv_full,
        preferred_element_type=jnp.float32,
    )
    pre = product + conv_bias
    act_mid, slope_mid, dalpha_mid = snake_parts(pre, alpha_mid)
    second = act_mid.astype(jnp.bfloat16)
    mix_term = lax.dot_general(
        second, cotangent, (((0,), (0,)), ((), ())), preferred_element_type=jnp.float32
    )
    second_gradient = lax.dot_general(
        cotangent, mix_full, (((1,), (1,)), ((), ())), preferred_element_type=jnp.float32
    )
    d_pre = (second_gradient * slope_mid).astype(jnp.bfloat16)
    convolution_part = lax.dot_general(
        unfolded, d_pre, (((0,), (0,)), ((), ())), preferred_element_type=jnp.float32
    )
    d_unf = lax.dot_general(
        d_pre,
        conv_full,
        (((1,), (1,)), ((), ())),
        preferred_element_type=jnp.float32,
    ).astype(jnp.bfloat16)
    d_first = jnp.zeros((rows, C), jnp.float32)
    for kernel_tap_index in range(TAPS):
        tap_offset = (kernel_tap_index - 3) * DILATION_SIZE
        piece = d_unf[:, kernel_tap_index * C : (kernel_tap_index + 1) * C].astype(jnp.float32)
        piece = jnp.where(same_clip_flags[kernel_tap_index][:, None], piece, jnp.zeros_like(piece))
        d_first = d_first + shift_rows(piece, -tap_offset, 0.0)
    in_grad = (cotangent.astype(jnp.float32) + d_first * slope_in).astype(jnp.bfloat16)
    vectors = jnp.stack(
        [
            jnp.sum(d_pre.astype(jnp.float32), axis=0),
            jnp.sum(cotangent.astype(jnp.float32), axis=0),
            jnp.sum(d_first * dalpha_in, axis=0),
            jnp.sum(second_gradient * dalpha_mid, axis=0),
        ]
    )
    sizes = [lax.axis_size(a) for a in FRAME_AXES]
    devices = 1
    for s in sizes:
        devices *= s
    conv_each = convolution_part.shape[0] // devices
    mix_each = mix_term.shape[0] // devices
    packed = jnp.concatenate(
        [
            convolution_part.reshape(devices, conv_each, C),
            mix_term.reshape(devices, mix_each, C),
        ],
        axis=1,
    )
    packed = packed.reshape(*sizes, conv_each + mix_each, C)
    order = [FRAME_AXES.index(a) for a in SCATTER_ORDER]
    packed = packed.transpose(*order, 4, 5).reshape(-1, C)
    for axis in SCATTER_ORDER:
        packed = lax.psum_scatter(packed, axis, scatter_dimension=0, tiled=True)
    conv_grad = packed[:conv_each]
    mix_grad = packed[conv_each:]
    vector_grad = lax.psum_scatter(vectors, FRAME_AXES, scatter_dimension=1, tiled=True)
    return (in_grad, conv_grad, mix_grad, vector_grad)


def solution(mesh):
    devices = mesh.devices
    xs = len({d.coords[0] for d in devices.flat})
    ys = len({d.coords[1] for d in devices.flat})
    dp, shard = devices.shape
    split = Mesh(devices.reshape(xs, ys, dp // (xs * ys), shard), FRAME_AXES)
    frames = P(FRAME_AXES, None)
    placed = (frames, frames, frames, P("z", None), P("z", None), P(), P(), P())
    return jax.shard_map(
        per_device,
        mesh=split,
        in_specs=placed,
        out_specs=(frames, frames, frames, P(None, FRAME_AXES)),
        check_vma=False,
    )
```

```python
import jax
import jax.numpy as jnp
from jax import lax
from jax.sharding import Mesh, PartitionSpec as P

C = 512
TAPS = 7
DILATION_SIZE = 9
FRAME_AXES = ("x", "y", "c", "z")
SCATTER_ORDER = ("c", "z", "y", "x")
EXTRA_COLUMNS = 128


def shift_rows(block, tap_offset, fill):
    rows = block.shape[0]
    shift_amount = min(abs(tap_offset), rows)
    if shift_amount == 0:
        return block
    edge_padding = jnp.full((shift_amount,) + block.shape[1:], fill, block.dtype)
    if tap_offset > 0:
        return jnp.concatenate([block[shift_amount:], edge_padding], axis=0)
    return jnp.concatenate([edge_padding, block[: rows - shift_amount]], axis=0)


def clip_masks(lengths_row, rows):
    clip_ends = jnp.cumsum(lengths_row)
    position = jnp.arange(rows, dtype=jnp.int32)
    clip_id = jnp.sum((position[:, None] >= clip_ends[None, :]).astype(jnp.int32), axis=1)
    result = []
    for kernel_tap_index in range(TAPS):
        tap_offset = (kernel_tap_index - 3) * DILATION_SIZE
        result.append(shift_rows(clip_id, tap_offset, -1) == clip_id)
    return result


def snake_parts(value, alpha):
    sine = jnp.sin(alpha * value)
    double = jnp.sin(2.0 * alpha * value)
    return (
        value + sine * sine / alpha,
        1.0 + double,
        value * double / alpha - sine * sine / (alpha * alpha),
    )


def per_device(
    audio, cotangent, clip_lengths, conv_weight, mix_weight, conv_bias, alpha_in, alpha_mid
):
    rows = audio.shape[0]
    same_clip_flags = clip_masks(clip_lengths[0], rows)
    conv_rows = conv_weight.shape[0]
    mix_rows = mix_weight.shape[0]
    both = jnp.concatenate([conv_weight, mix_weight], axis=0)
    gathered = lax.all_gather(both, "z", axis=0, tiled=True)
    gathered = gathered.reshape(-1, conv_rows + mix_rows, C)
    conv_full = gathered[:, :conv_rows].reshape(-1, C)
    mix_full = gathered[:, conv_rows:].reshape(-1, C)
    audio_f = audio.astype(jnp.float32)
    act_in, slope_in, dalpha_in = snake_parts(audio_f, alpha_in)
    first = act_in.astype(jnp.bfloat16)
    columns = []
    for kernel_tap_index in range(TAPS):
        tap_offset = (kernel_tap_index - 3) * DILATION_SIZE
        moved = shift_rows(first, tap_offset, 0)
        columns.append(
            jnp.where(same_clip_flags[kernel_tap_index][:, None], moved, jnp.zeros_like(moved))
        )
    unfolded = jnp.concatenate(columns, axis=1)
    product = jnp.dot(
        unfolded,
        conv_full,
        preferred_element_type=jnp.float32,
    )
    pre = product + conv_bias
    act_mid, slope_mid, dalpha_mid = snake_parts(pre, alpha_mid)
    second = act_mid.astype(jnp.bfloat16)
    mix_term = lax.dot_general(
        second, cotangent, (((0,), (0,)), ((), ())), preferred_element_type=jnp.float32
    )
    second_gradient = lax.dot_general(
        cotangent, mix_full, (((1,), (1,)), ((), ())), preferred_element_type=jnp.float32
    )
    d_pre = (second_gradient * slope_mid).astype(jnp.bfloat16)
    convolution_part = lax.dot_general(
        unfolded, d_pre, (((0,), (0,)), ((), ())), preferred_element_type=jnp.float32
    )
    d_unf = lax.dot_general(
        d_pre,
        conv_full,
        (((1,), (1,)), ((), ())),
        preferred_element_type=jnp.float32,
    ).astype(jnp.bfloat16)
    d_first = jnp.zeros((rows, C), jnp.float32)
    for kernel_tap_index in range(TAPS):
        tap_offset = (kernel_tap_index - 3) * DILATION_SIZE
        piece = d_unf[:, kernel_tap_index * C : (kernel_tap_index + 1) * C].astype(jnp.float32)
        piece = jnp.where(same_clip_flags[kernel_tap_index][:, None], piece, jnp.zeros_like(piece))
        d_first = d_first + shift_rows(piece, -tap_offset, 0.0)
    in_grad = (cotangent.astype(jnp.float32) + d_first * slope_in).astype(jnp.bfloat16)
    vectors = jnp.stack(
        [
            jnp.sum(d_pre.astype(jnp.float32), axis=0),
            jnp.sum(cotangent.astype(jnp.float32), axis=0),
            jnp.sum(d_first * dalpha_in, axis=0),
            jnp.sum(second_gradient * dalpha_mid, axis=0),
        ]
    )
    sizes = [lax.axis_size(a) for a in FRAME_AXES]
    devices = 1
    for s in sizes:
        devices *= s
    conv_each = convolution_part.shape[0] // devices
    mix_each = mix_term.shape[0] // devices
    packed = jnp.concatenate(
        [
            convolution_part.reshape(devices, conv_each, C),
            mix_term.reshape(devices, mix_each, C),
        ],
        axis=1,
    )
    packed = packed.reshape(*sizes, conv_each + mix_each, C)
    order = [FRAME_AXES.index(a) for a in SCATTER_ORDER]
    packed = packed.transpose(*order, 4, 5).reshape(-1, C)
    first_axis, *rest = SCATTER_ORDER
    packed = lax.psum_scatter(packed, first_axis, scatter_dimension=0, tiled=True)
    vectors = lax.psum(vectors, first_axis)
    block = conv_each + mix_each
    held = packed.shape[0] // block
    share = vectors.shape[1] // devices
    vec_blocks = vectors.reshape(4, devices, share).transpose(1, 0, 2).reshape(*sizes, 4 * share)
    order_rest = [FRAME_AXES.index(a) for a in rest]
    mine = lax.axis_index(first_axis)
    vec_blocks = jnp.take(vec_blocks, mine, axis=FRAME_AXES.index(first_axis))
    kept = [FRAME_AXES.index(a) for a in FRAME_AXES if a != first_axis]
    vec_blocks = vec_blocks.transpose(*[kept.index(o) for o in order_rest], len(kept))
    vec_blocks = vec_blocks.reshape(held, 4 * share)
    extra = jnp.zeros((held, block, EXTRA_COLUMNS), jnp.float32)
    extra = extra.at[:, 0, : 4 * share].set(vec_blocks)
    packed = jnp.concatenate([packed.reshape(held, block, C), extra], axis=2)
    packed = packed.reshape(held * block, C + EXTRA_COLUMNS).astype(jnp.bfloat16)
    for i, axis in enumerate(rest):
        packed = lax.psum_scatter(packed, axis, scatter_dimension=0, tiled=True)
        if i == 0:
            packed = packed.astype(jnp.float32)
    conv_grad = packed[:conv_each, :C]
    mix_grad = packed[conv_each:, :C]
    vector_grad = packed[0, C : C + 4 * share].reshape(4, share)
    return (in_grad, conv_grad, mix_grad, vector_grad)


def solution(mesh):
    devices = mesh.devices
    xs = len({d.coords[0] for d in devices.flat})
    ys = len({d.coords[1] for d in devices.flat})
    dp, shard = devices.shape
    split = Mesh(devices.reshape(xs, ys, dp // (xs * ys), shard), FRAME_AXES)
    frames = P(FRAME_AXES, None)
    placed = (frames, frames, frames, P("z", None), P("z", None), P(), P(), P())
    return jax.shard_map(
        per_device,
        mesh=split,
        in_specs=placed,
        out_specs=(frames, frames, frames, P(None, FRAME_AXES)),
        check_vma=False,
    )
```

```python
import jax
import jax.numpy as jnp
from jax import lax
from jax.sharding import Mesh, PartitionSpec as P

C = 512
TAPS = 7
DILATION_SIZE = 9
FRAME_AXES = ("x", "y", "c", "z")
SCATTER_ORDER = ("c", "z", "y", "x")
EXTRA_COLUMNS = 128


def shift_rows(block, tap_offset, fill):
    rows = block.shape[0]
    shift_amount = min(abs(tap_offset), rows)
    if shift_amount == 0:
        return block
    edge_padding = jnp.full((shift_amount,) + block.shape[1:], fill, block.dtype)
    if tap_offset > 0:
        return jnp.concatenate([block[shift_amount:], edge_padding], axis=0)
    return jnp.concatenate([edge_padding, block[: rows - shift_amount]], axis=0)


def clip_masks(lengths_row, rows):
    clip_ends = jnp.cumsum(lengths_row)
    position = jnp.arange(rows, dtype=jnp.int32)
    clip_id = jnp.sum((position[:, None] >= clip_ends[None, :]).astype(jnp.int32), axis=1)
    result = []
    for kernel_tap_index in range(TAPS):
        tap_offset = (kernel_tap_index - 3) * DILATION_SIZE
        result.append(shift_rows(clip_id, tap_offset, -1) == clip_id)
    return result


def snake_parts(value, alpha):
    sine = jnp.sin(alpha * value)
    double = jnp.sin(2.0 * alpha * value)
    return (
        value + sine * sine / alpha,
        1.0 + double,
        value * double / alpha - sine * sine / (alpha * alpha),
    )


def permute_scatter(value, axis):
    n = lax.axis_size(axis)
    me = lax.axis_index(axis)
    each = value.shape[0] // n
    total = lax.dynamic_slice_in_dim(value, me * each, each)
    for step in range(1, n):
        chunk = lax.dynamic_slice_in_dim(value, ((me + step) % n) * each, each)
        total = total + lax.ppermute(chunk, axis, [(j, (j + step) % n) for j in range(n)])
    return total


def per_device(
    audio, cotangent, clip_lengths, conv_weight, mix_weight, conv_bias, alpha_in, alpha_mid
):
    rows = audio.shape[0]
    same_clip_flags = clip_masks(clip_lengths[0], rows)
    conv_rows = conv_weight.shape[0]
    mix_rows = mix_weight.shape[0]
    both = jnp.concatenate([conv_weight, mix_weight], axis=0)
    gathered = lax.all_gather(both, "z", axis=0, tiled=True)
    gathered = gathered.reshape(-1, conv_rows + mix_rows, C)
    conv_full = gathered[:, :conv_rows].reshape(-1, C)
    mix_full = gathered[:, conv_rows:].reshape(-1, C)
    audio_f = audio.astype(jnp.float32)
    act_in, slope_in, dalpha_in = snake_parts(audio_f, alpha_in)
    first = act_in.astype(jnp.bfloat16)
    columns = []
    for kernel_tap_index in range(TAPS):
        tap_offset = (kernel_tap_index - 3) * DILATION_SIZE
        moved = shift_rows(first, tap_offset, 0)
        columns.append(
            jnp.where(same_clip_flags[kernel_tap_index][:, None], moved, jnp.zeros_like(moved))
        )
    unfolded = jnp.concatenate(columns, axis=1)
    product = jnp.dot(
        unfolded,
        conv_full,
        preferred_element_type=jnp.float32,
    )
    pre = product + conv_bias
    act_mid, slope_mid, dalpha_mid = snake_parts(pre, alpha_mid)
    second = act_mid.astype(jnp.bfloat16)
    mix_term = lax.dot_general(
        second, cotangent, (((0,), (0,)), ((), ())), preferred_element_type=jnp.float32
    )
    second_gradient = lax.dot_general(
        cotangent, mix_full, (((1,), (1,)), ((), ())), preferred_element_type=jnp.float32
    )
    d_pre = (second_gradient * slope_mid).astype(jnp.bfloat16)
    convolution_part = lax.dot_general(
        unfolded, d_pre, (((0,), (0,)), ((), ())), preferred_element_type=jnp.float32
    )
    d_unf = lax.dot_general(
        d_pre,
        conv_full,
        (((1,), (1,)), ((), ())),
        preferred_element_type=jnp.float32,
    ).astype(jnp.bfloat16)
    d_first = jnp.zeros((rows, C), jnp.float32)
    for kernel_tap_index in range(TAPS):
        tap_offset = (kernel_tap_index - 3) * DILATION_SIZE
        piece = d_unf[:, kernel_tap_index * C : (kernel_tap_index + 1) * C].astype(jnp.float32)
        piece = jnp.where(same_clip_flags[kernel_tap_index][:, None], piece, jnp.zeros_like(piece))
        d_first = d_first + shift_rows(piece, -tap_offset, 0.0)
    in_grad = (cotangent.astype(jnp.float32) + d_first * slope_in).astype(jnp.bfloat16)
    vectors = jnp.stack(
        [
            jnp.sum(d_pre.astype(jnp.float32), axis=0),
            jnp.sum(cotangent.astype(jnp.float32), axis=0),
            jnp.sum(d_first * dalpha_in, axis=0),
            jnp.sum(second_gradient * dalpha_mid, axis=0),
        ]
    )
    sizes = [lax.axis_size(a) for a in FRAME_AXES]
    devices = 1
    for s in sizes:
        devices *= s
    conv_each = convolution_part.shape[0] // devices
    mix_each = mix_term.shape[0] // devices
    packed = jnp.concatenate(
        [
            convolution_part.reshape(devices, conv_each, C),
            mix_term.reshape(devices, mix_each, C),
        ],
        axis=1,
    )
    packed = packed.reshape(*sizes, conv_each + mix_each, C)
    order = [FRAME_AXES.index(a) for a in SCATTER_ORDER]
    packed = packed.transpose(*order, 4, 5).reshape(-1, C)
    first_axis, *rest = SCATTER_ORDER
    packed = lax.psum_scatter(packed, first_axis, scatter_dimension=0, tiled=True)
    vectors = lax.psum(vectors, first_axis)
    block = conv_each + mix_each
    held = packed.shape[0] // block
    share = vectors.shape[1] // devices
    vec_blocks = vectors.reshape(4, devices, share).transpose(1, 0, 2).reshape(*sizes, 4 * share)
    order_rest = [FRAME_AXES.index(a) for a in rest]
    mine = lax.axis_index(first_axis)
    vec_blocks = jnp.take(vec_blocks, mine, axis=FRAME_AXES.index(first_axis))
    kept = [FRAME_AXES.index(a) for a in FRAME_AXES if a != first_axis]
    vec_blocks = vec_blocks.transpose(*[kept.index(o) for o in order_rest], len(kept))
    vec_blocks = vec_blocks.reshape(held, 4 * share)
    extra = jnp.zeros((held, block, EXTRA_COLUMNS), jnp.float32)
    extra = extra.at[:, 0, : 4 * share].set(vec_blocks)
    packed = jnp.concatenate([packed.reshape(held, block, C), extra], axis=2)
    packed = packed.reshape(held * block, C + EXTRA_COLUMNS).astype(jnp.bfloat16)
    packed = lax.psum_scatter(packed, rest[0], scatter_dimension=0, tiled=True)
    packed = packed.astype(jnp.float32)
    for axis in rest[1:]:
        packed = permute_scatter(packed, axis)
    conv_grad = packed[:conv_each, :C]
    mix_grad = packed[conv_each:, :C]
    vector_grad = packed[0, C : C + 4 * share].reshape(4, share)
    return (in_grad, conv_grad, mix_grad, vector_grad)


def solution(mesh):
    devices = mesh.devices
    xs = len({d.coords[0] for d in devices.flat})
    ys = len({d.coords[1] for d in devices.flat})
    dp, shard = devices.shape
    split = Mesh(devices.reshape(xs, ys, dp // (xs * ys), shard), FRAME_AXES)
    frames = P(FRAME_AXES, None)
    placed = (frames, frames, frames, P("z", None), P("z", None), P(), P(), P())
    return jax.shard_map(
        per_device,
        mesh=split,
        in_specs=placed,
        out_specs=(frames, frames, frames, P(None, FRAME_AXES)),
        check_vma=False,
    )
```

```python
import jax
import jax.numpy as jnp
from jax import lax
from jax.sharding import Mesh, PartitionSpec as P

C = 512
TAPS = 7
DILATION_SIZE = 9
FRAME_AXES = ("x", "y", "c", "z")
SCATTER_ORDER = ("c", "z", "y", "x")
EXTRA_COLUMNS = 128


def shift_rows(block, tap_offset, fill):
    rows = block.shape[0]
    shift_amount = min(abs(tap_offset), rows)
    if shift_amount == 0:
        return block
    edge_padding = jnp.full((shift_amount,) + block.shape[1:], fill, block.dtype)
    if tap_offset > 0:
        return jnp.concatenate([block[shift_amount:], edge_padding], axis=0)
    return jnp.concatenate([edge_padding, block[: rows - shift_amount]], axis=0)


def clip_masks(lengths_row, rows):
    clip_ends = jnp.cumsum(lengths_row)
    position = jnp.arange(rows, dtype=jnp.int32)
    clip_id = jnp.sum((position[:, None] >= clip_ends[None, :]).astype(jnp.int32), axis=1)
    result = []
    for kernel_tap_index in range(TAPS):
        tap_offset = (kernel_tap_index - 3) * DILATION_SIZE
        result.append(shift_rows(clip_id, tap_offset, -1) == clip_id)
    return result


def snake_parts(value, alpha):
    sine = jnp.sin(alpha * value)
    double = jnp.sin(2.0 * alpha * value)
    return (
        value + sine * sine / alpha,
        1.0 + double,
        value * double / alpha - sine * sine / (alpha * alpha),
    )


def permute_scatter(value, axis):
    n = lax.axis_size(axis)
    me = lax.axis_index(axis)
    each = value.shape[0] // n
    total = lax.dynamic_slice_in_dim(value, me * each, each)
    for step in range(1, n):
        chunk = lax.dynamic_slice_in_dim(value, ((me + step) % n) * each, each)
        total = total + lax.ppermute(chunk, axis, [(j, (j + step) % n) for j in range(n)])
    return total


def per_device(
    audio, cotangent, clip_lengths, conv_weight, mix_weight, conv_bias, alpha_in, alpha_mid
):
    rows = audio.shape[0]
    same_clip_flags = clip_masks(clip_lengths[0], rows)
    conv_rows = conv_weight.shape[0]
    mix_rows = mix_weight.shape[0]
    both = jnp.concatenate([conv_weight, mix_weight], axis=0)
    gathered = lax.all_gather(both, "z", axis=0, tiled=True)
    gathered = gathered.reshape(-1, conv_rows + mix_rows, C)
    conv_full = gathered[:, :conv_rows].reshape(-1, C)
    mix_full = gathered[:, conv_rows:].reshape(-1, C)
    audio_f = audio.astype(jnp.float32)
    act_in, slope_in, dalpha_in = snake_parts(audio_f, alpha_in)
    first = act_in.astype(jnp.bfloat16)
    columns = []
    for kernel_tap_index in range(TAPS):
        tap_offset = (kernel_tap_index - 3) * DILATION_SIZE
        moved = shift_rows(first, tap_offset, 0)
        columns.append(
            jnp.where(same_clip_flags[kernel_tap_index][:, None], moved, jnp.zeros_like(moved))
        )
    unfolded = jnp.concatenate(columns, axis=1)
    product = jnp.dot(
        unfolded,
        conv_full,
        preferred_element_type=jnp.float32,
    )
    pre = product + conv_bias
    act_mid, slope_mid, dalpha_mid = snake_parts(pre, alpha_mid)
    second = act_mid.astype(jnp.bfloat16)
    second_gradient = lax.dot_general(
        cotangent, mix_full, (((1,), (1,)), ((), ())), preferred_element_type=jnp.float32
    )
    d_pre = (second_gradient * slope_mid).astype(jnp.bfloat16)
    d_unf = lax.dot_general(
        d_pre,
        conv_full,
        (((1,), (1,)), ((), ())),
        preferred_element_type=jnp.float32,
    ).astype(jnp.bfloat16)
    d_first = jnp.zeros((rows, C), jnp.float32)
    for kernel_tap_index in range(TAPS):
        tap_offset = (kernel_tap_index - 3) * DILATION_SIZE
        piece = d_unf[:, kernel_tap_index * C : (kernel_tap_index + 1) * C].astype(jnp.float32)
        piece = jnp.where(same_clip_flags[kernel_tap_index][:, None], piece, jnp.zeros_like(piece))
        d_first = d_first + shift_rows(piece, -tap_offset, 0.0)
    in_grad = (cotangent.astype(jnp.float32) + d_first * slope_in).astype(jnp.bfloat16)
    vectors = jnp.stack(
        [
            jnp.sum(d_pre.astype(jnp.float32), axis=0),
            jnp.sum(cotangent.astype(jnp.float32), axis=0),
            jnp.sum(d_first * dalpha_in, axis=0),
            jnp.sum(second_gradient * dalpha_mid, axis=0),
        ]
    )
    sizes = [lax.axis_size(a) for a in FRAME_AXES]
    devices = 1
    for s in sizes:
        devices *= s
    conv_each = unfolded.shape[1] // devices
    mix_each = second.shape[1] // devices
    order = [FRAME_AXES.index(a) for a in SCATTER_ORDER]

    def lay_out(left):
        left = jnp.concatenate(left, axis=2).reshape(rows, *sizes, conv_each + mix_each)
        return left.transpose(0, *[o + 1 for o in order], 5).reshape(rows, -1)

    conv_lhs = lay_out([unfolded.reshape(rows, devices, conv_each), jnp.zeros((rows, devices, mix_each), unfolded.dtype)])
    mix_lhs = lay_out([jnp.zeros((rows, devices, conv_each), second.dtype), second.reshape(rows, devices, mix_each)])
    packed = lax.dot_general(
        jnp.concatenate([conv_lhs, mix_lhs], axis=0),
        jnp.concatenate([d_pre, cotangent], axis=0),
        (((0,), (0,)), ((), ())),
        preferred_element_type=jnp.float32,
    )
    first_axis, *rest = SCATTER_ORDER
    packed = lax.psum_scatter(packed, first_axis, scatter_dimension=0, tiled=True)
    vectors = lax.psum(vectors, first_axis)
    block = conv_each + mix_each
    held = packed.shape[0] // block
    share = vectors.shape[1] // devices
    vec_blocks = vectors.reshape(4, devices, share).transpose(1, 0, 2).reshape(*sizes, 4 * share)
    order_rest = [FRAME_AXES.index(a) for a in rest]
    mine = lax.axis_index(first_axis)
    vec_blocks = jnp.take(vec_blocks, mine, axis=FRAME_AXES.index(first_axis))
    kept = [FRAME_AXES.index(a) for a in FRAME_AXES if a != first_axis]
    vec_blocks = vec_blocks.transpose(*[kept.index(o) for o in order_rest], len(kept))
    vec_blocks = vec_blocks.reshape(held, 4 * share)
    extra = jnp.zeros((held, block, EXTRA_COLUMNS), jnp.float32)
    extra = extra.at[:, 0, : 4 * share].set(vec_blocks)
    packed = jnp.concatenate([packed.reshape(held, block, C), extra], axis=2)
    packed = packed.reshape(held * block, C + EXTRA_COLUMNS).astype(jnp.bfloat16)
    packed = lax.psum_scatter(packed, rest[0], scatter_dimension=0, tiled=True)
    packed = packed.astype(jnp.float32)
    for axis in rest[1:]:
        packed = permute_scatter(packed, axis)
    conv_grad = packed[:conv_each, :C]
    mix_grad = packed[conv_each:, :C]
    vector_grad = packed[0, C : C + 4 * share].reshape(4, share)
    return (in_grad, conv_grad, mix_grad, vector_grad)


def solution(mesh):
    devices = mesh.devices
    xs = len({d.coords[0] for d in devices.flat})
    ys = len({d.coords[1] for d in devices.flat})
    dp, shard = devices.shape
    split = Mesh(devices.reshape(xs, ys, dp // (xs * ys), shard), FRAME_AXES)
    frames = P(FRAME_AXES)
    placed = (frames, frames, frames, P("z", None), P("z", None), P(), P(), P())
    return jax.shard_map(
        per_device,
        mesh=split,
        in_specs=placed,
        out_specs=(frames, frames, frames, P(None, FRAME_AXES)),
        check_vma=False,
    )
```

```python
import jax
import jax.numpy as jnp
from jax import lax
from jax.sharding import Mesh, PartitionSpec as P

C = 512
TAPS = 7
DILATION_SIZE = 9
FRAME_AXES = ("x", "y", "c", "z")
SCATTER_ORDER = ("c", "z", "x", "y")
EXTRA_COLUMNS = 128


def shift_rows(block, tap_offset, fill):
    rows = block.shape[0]
    shift_amount = min(abs(tap_offset), rows)
    if shift_amount == 0:
        return block
    edge_padding = jnp.full((shift_amount,) + block.shape[1:], fill, block.dtype)
    if tap_offset > 0:
        return jnp.concatenate([block[shift_amount:], edge_padding], axis=0)
    return jnp.concatenate([edge_padding, block[: rows - shift_amount]], axis=0)


def clip_masks(lengths_row, rows):
    clip_ends = jnp.cumsum(lengths_row)
    position = jnp.arange(rows, dtype=jnp.int32)
    clip_id = jnp.sum((position[:, None] >= clip_ends[None, :]).astype(jnp.int32), axis=1)
    result = []
    for kernel_tap_index in range(TAPS):
        tap_offset = (kernel_tap_index - 3) * DILATION_SIZE
        result.append(shift_rows(clip_id, tap_offset, -1) == clip_id)
    return result


def snake_parts(value, alpha):
    sine = jnp.sin(alpha * value)
    double = jnp.sin(2.0 * alpha * value)
    return (
        value + sine * sine / alpha,
        1.0 + double,
        value * double / alpha - sine * sine / (alpha * alpha),
    )


def permute_scatter(value, axis):
    n = lax.axis_size(axis)
    me = lax.axis_index(axis)
    each = value.shape[0] // n
    total = lax.dynamic_slice_in_dim(value, me * each, each)
    for step in range(1, n):
        chunk = lax.dynamic_slice_in_dim(value, ((me + step) % n) * each, each)
        total = total + lax.ppermute(chunk, axis, [(j, (j + step) % n) for j in range(n)])
    return total


def per_device(
    audio, cotangent, clip_lengths, conv_weight, mix_weight, conv_bias, alpha_in, alpha_mid
):
    rows = audio.shape[0]
    same_clip_flags = clip_masks(clip_lengths[0], rows)
    conv_rows = conv_weight.shape[0]
    mix_rows = mix_weight.shape[0]
    both = jnp.concatenate([conv_weight, mix_weight], axis=0)
    gathered = lax.all_gather(both, "z", axis=0, tiled=True)
    gathered = gathered.reshape(-1, conv_rows + mix_rows, C)
    conv_full = gathered[:, :conv_rows].reshape(-1, C)
    mix_full = gathered[:, conv_rows:].reshape(-1, C)
    audio_f = audio.astype(jnp.float32)
    act_in, slope_in, dalpha_in = snake_parts(audio_f, alpha_in)
    first = act_in.astype(jnp.bfloat16)
    columns = []
    for kernel_tap_index in range(TAPS):
        tap_offset = (kernel_tap_index - 3) * DILATION_SIZE
        moved = shift_rows(first, tap_offset, 0)
        columns.append(
            jnp.where(same_clip_flags[kernel_tap_index][:, None], moved, jnp.zeros_like(moved))
        )
    unfolded = jnp.concatenate(columns, axis=1)
    product = jnp.dot(
        unfolded,
        conv_full,
        preferred_element_type=jnp.float32,
    )
    pre = product + conv_bias
    act_mid, slope_mid, dalpha_mid = snake_parts(pre, alpha_mid)
    second = act_mid.astype(jnp.bfloat16)
    second_gradient = lax.dot_general(
        cotangent, mix_full, (((1,), (1,)), ((), ())), preferred_element_type=jnp.float32
    )
    d_pre = (second_gradient * slope_mid).astype(jnp.bfloat16)
    d_unf = lax.dot_general(
        d_pre,
        conv_full,
        (((1,), (1,)), ((), ())),
        preferred_element_type=jnp.float32,
    ).astype(jnp.bfloat16)
    d_first = jnp.zeros((rows, C), jnp.float32)
    for kernel_tap_index in range(TAPS):
        tap_offset = (kernel_tap_index - 3) * DILATION_SIZE
        piece = d_unf[:, kernel_tap_index * C : (kernel_tap_index + 1) * C].astype(jnp.float32)
        piece = jnp.where(same_clip_flags[kernel_tap_index][:, None], piece, jnp.zeros_like(piece))
        d_first = d_first + shift_rows(piece, -tap_offset, 0.0)
    in_grad = (cotangent.astype(jnp.float32) + d_first * slope_in).astype(jnp.bfloat16)
    vectors = jnp.stack(
        [
            jnp.sum(d_pre.astype(jnp.float32), axis=0),
            jnp.sum(cotangent.astype(jnp.float32), axis=0),
            jnp.sum(d_first * dalpha_in, axis=0),
            jnp.sum(second_gradient * dalpha_mid, axis=0),
        ]
    )
    sizes = [lax.axis_size(a) for a in FRAME_AXES]
    devices = 1
    for s in sizes:
        devices *= s
    conv_each = unfolded.shape[1] // devices
    mix_each = second.shape[1] // devices
    order = [FRAME_AXES.index(a) for a in SCATTER_ORDER]

    def lay_out(left):
        left = jnp.concatenate(left, axis=2).reshape(rows, *sizes, conv_each + mix_each)
        return left.transpose(0, *[o + 1 for o in order], 5).reshape(rows, -1)

    conv_lhs = lay_out([unfolded.reshape(rows, devices, conv_each), jnp.zeros((rows, devices, mix_each), unfolded.dtype)])
    mix_lhs = lay_out([jnp.zeros((rows, devices, conv_each), second.dtype), second.reshape(rows, devices, mix_each)])
    packed = lax.dot_general(
        jnp.concatenate([conv_lhs, mix_lhs], axis=0),
        jnp.concatenate([d_pre, cotangent], axis=0),
        (((0,), (0,)), ((), ())),
        preferred_element_type=jnp.float32,
    )
    first_axis, *rest = SCATTER_ORDER
    packed = lax.psum_scatter(packed, first_axis, scatter_dimension=0, tiled=True)
    vectors = lax.psum(vectors, first_axis)
    block = conv_each + mix_each
    held = packed.shape[0] // block
    share = vectors.shape[1] // devices
    vec_blocks = vectors.reshape(4, devices, share).transpose(1, 0, 2).reshape(*sizes, 4 * share)
    order_rest = [FRAME_AXES.index(a) for a in rest]
    mine = lax.axis_index(first_axis)
    vec_blocks = jnp.take(vec_blocks, mine, axis=FRAME_AXES.index(first_axis))
    kept = [FRAME_AXES.index(a) for a in FRAME_AXES if a != first_axis]
    vec_blocks = vec_blocks.transpose(*[kept.index(o) for o in order_rest], len(kept))
    vec_blocks = vec_blocks.reshape(held, 4 * share)
    extra = jnp.zeros((held, block, EXTRA_COLUMNS), jnp.float32)
    extra = extra.at[:, 0, : 4 * share].set(vec_blocks)
    packed = jnp.concatenate([packed.reshape(held, block, C), extra], axis=2)
    packed = packed.reshape(held * block, C + EXTRA_COLUMNS).astype(jnp.bfloat16)
    packed = lax.psum_scatter(packed, rest[0], scatter_dimension=0, tiled=True)
    packed = packed.astype(jnp.float32)
    packed = permute_scatter(packed, tuple(rest[1:]))
    conv_grad = packed[:conv_each, :C]
    mix_grad = packed[conv_each:, :C]
    vector_grad = packed[0, C : C + 4 * share].reshape(4, share)
    return (in_grad, conv_grad, mix_grad, vector_grad)


def solution(mesh):
    devices = mesh.devices
    xs = len({d.coords[0] for d in devices.flat})
    ys = len({d.coords[1] for d in devices.flat})
    dp, shard = devices.shape
    split = Mesh(devices.reshape(xs, ys, dp // (xs * ys), shard), FRAME_AXES)
    frames = P(FRAME_AXES)
    placed = (frames, frames, frames, P("z", None), P("z", None), P(), P(), P())
    return jax.shard_map(
        per_device,
        mesh=split,
        in_specs=placed,
        out_specs=(frames, frames, frames, P(None, FRAME_AXES)),
        check_vma=False,
    )
```

```python
import jax
import jax.numpy as jnp
from jax import lax
from jax.sharding import Mesh, PartitionSpec as P

C = 512
TAPS = 7
DILATION_SIZE = 9
FRAME_AXES = ("x", "y", "c", "z")
SCATTER_ORDER = ("c", "z", "y", "x")
EXTRA_COLUMNS = 128


def shift_rows(block, tap_offset, fill):
    rows = block.shape[0]
    shift_amount = min(abs(tap_offset), rows)
    if shift_amount == 0:
        return block
    edge_padding = jnp.full((shift_amount,) + block.shape[1:], fill, block.dtype)
    if tap_offset > 0:
        return jnp.concatenate([block[shift_amount:], edge_padding], axis=0)
    return jnp.concatenate([edge_padding, block[: rows - shift_amount]], axis=0)


def clip_masks(lengths_row, rows):
    clip_ends = jnp.cumsum(lengths_row)
    position = jnp.arange(rows, dtype=jnp.int32)
    clip_id = jnp.sum((position[:, None] >= clip_ends[None, :]).astype(jnp.int32), axis=1)
    result = []
    for kernel_tap_index in range(TAPS):
        tap_offset = (kernel_tap_index - 3) * DILATION_SIZE
        result.append(shift_rows(clip_id, tap_offset, -1) == clip_id)
    return result


def snake_parts(value, alpha):
    sine = jnp.sin(alpha * value)
    double = jnp.sin(2.0 * alpha * value)
    return (
        value + sine * sine / alpha,
        1.0 + double,
        value * double / alpha - sine * sine / (alpha * alpha),
    )


def permute_scatter(value, axis):
    n = lax.axis_size(axis)
    me = lax.axis_index(axis)
    each = value.shape[0] // n
    total = lax.dynamic_slice_in_dim(value, me * each, each)
    for step in range(1, n):
        chunk = lax.dynamic_slice_in_dim(value, ((me + step) % n) * each, each)
        total = total + lax.ppermute(chunk, axis, [(j, (j + step) % n) for j in range(n)])
    return total


def per_device(
    audio, cotangent, clip_lengths, conv_weight, mix_weight, conv_bias, alpha_in, alpha_mid
):
    rows = audio.shape[0]
    same_clip_flags = clip_masks(clip_lengths[0], rows)
    conv_rows = conv_weight.shape[0]
    mix_rows = mix_weight.shape[0]
    both = jnp.concatenate([conv_weight, mix_weight], axis=0)
    gathered = lax.all_gather(both, "z", axis=0, tiled=True)
    gathered = gathered.reshape(-1, conv_rows + mix_rows, C)
    conv_full = gathered[:, :conv_rows].reshape(-1, C)
    mix_full = gathered[:, conv_rows:].reshape(-1, C)
    audio_f = audio.astype(jnp.float32)
    act_in, slope_in, dalpha_in = snake_parts(audio_f, alpha_in)
    first = act_in.astype(jnp.bfloat16)
    columns = []
    for kernel_tap_index in range(TAPS):
        tap_offset = (kernel_tap_index - 3) * DILATION_SIZE
        moved = shift_rows(first, tap_offset, 0)
        columns.append(
            jnp.where(same_clip_flags[kernel_tap_index][:, None], moved, jnp.zeros_like(moved))
        )
    unfolded = jnp.concatenate(columns, axis=1)
    product = jnp.dot(
        unfolded,
        conv_full,
        preferred_element_type=jnp.float32,
    )
    pre = product + conv_bias
    act_mid, slope_mid, dalpha_mid = snake_parts(pre, alpha_mid)
    second = act_mid.astype(jnp.bfloat16)
    second_gradient = lax.dot_general(
        cotangent, mix_full, (((1,), (1,)), ((), ())), preferred_element_type=jnp.float32
    )
    d_pre = (second_gradient * slope_mid).astype(jnp.bfloat16)
    d_unf = lax.dot_general(
        d_pre,
        conv_full,
        (((1,), (1,)), ((), ())),
        preferred_element_type=jnp.float32,
    ).astype(jnp.bfloat16)
    d_first = jnp.zeros((rows, C), jnp.float32)
    for kernel_tap_index in range(TAPS):
        tap_offset = (kernel_tap_index - 3) * DILATION_SIZE
        piece = d_unf[:, kernel_tap_index * C : (kernel_tap_index + 1) * C].astype(jnp.float32)
        piece = jnp.where(same_clip_flags[kernel_tap_index][:, None], piece, jnp.zeros_like(piece))
        d_first = d_first + shift_rows(piece, -tap_offset, 0.0)
    in_grad = (cotangent.astype(jnp.float32) + d_first * slope_in).astype(jnp.bfloat16)
    vectors = jnp.stack(
        [
            jnp.sum(d_pre.astype(jnp.float32), axis=0),
            jnp.sum(cotangent.astype(jnp.float32), axis=0),
            jnp.sum(d_first * dalpha_in, axis=0),
            jnp.sum(second_gradient * dalpha_mid, axis=0),
        ]
    )
    sizes = [lax.axis_size(a) for a in FRAME_AXES]
    devices = 1
    for s in sizes:
        devices *= s
    conv_each = unfolded.shape[1] // devices
    mix_each = second.shape[1] // devices
    order = [FRAME_AXES.index(a) for a in SCATTER_ORDER]

    def lay_out(left):
        left = jnp.concatenate(left, axis=2).reshape(rows, *sizes, conv_each + mix_each)
        return left.transpose(0, *[o + 1 for o in order], 5).reshape(rows, -1)

    conv_lhs = lay_out([unfolded.reshape(rows, devices, conv_each), jnp.zeros((rows, devices, mix_each), unfolded.dtype)])
    mix_lhs = lay_out([jnp.zeros((rows, devices, conv_each), second.dtype), second.reshape(rows, devices, mix_each)])
    packed = lax.dot_general(
        jnp.concatenate([conv_lhs, mix_lhs], axis=0),
        jnp.concatenate([d_pre, cotangent], axis=0),
        (((0,), (0,)), ((), ())),
        preferred_element_type=jnp.float32,
    )
    first_axis, second_axis, *rest = SCATTER_ORDER
    packed = lax.psum_scatter(packed, first_axis, scatter_dimension=0, tiled=True)
    packed = lax.psum_scatter(packed.astype(jnp.bfloat16), second_axis, scatter_dimension=0, tiled=True)
    packed = packed.astype(jnp.float32)
    vectors = lax.psum(vectors, first_axis)
    vectors = lax.psum(vectors, second_axis)
    block = conv_each + mix_each
    held = packed.shape[0] // block
    share = vectors.shape[1] // devices
    vec_blocks = vectors.reshape(4, devices, share).transpose(1, 0, 2).reshape(*sizes, 4 * share)
    kept_names = list(FRAME_AXES)
    for axis in (first_axis, second_axis):
        position = kept_names.index(axis)
        vec_blocks = jnp.take(vec_blocks, lax.axis_index(axis), axis=position)
        kept_names.pop(position)
    vec_blocks = vec_blocks.transpose(*[kept_names.index(a) for a in rest], len(kept_names))
    vec_blocks = vec_blocks.reshape(held, 4 * share)
    extra = jnp.zeros((held, block, EXTRA_COLUMNS), jnp.float32)
    extra = extra.at[:, 0, : 4 * share].set(vec_blocks)
    packed = jnp.concatenate([packed.reshape(held, block, C), extra], axis=2)
    packed = packed.reshape(held * block, C + EXTRA_COLUMNS)
    for axis in rest:
        packed = permute_scatter(packed, axis)
    conv_grad = packed[:conv_each, :C]
    mix_grad = packed[conv_each:, :C]
    vector_grad = packed[0, C : C + 4 * share].reshape(4, share)
    return (in_grad, conv_grad, mix_grad, vector_grad)


def solution(mesh):
    devices = mesh.devices
    xs = len({d.coords[0] for d in devices.flat})
    ys = len({d.coords[1] for d in devices.flat})
    dp, shard = devices.shape
    split = Mesh(devices.reshape(xs, ys, dp // (xs * ys), shard), FRAME_AXES)
    frames = P(FRAME_AXES)
    placed = (frames, frames, frames, P("z", None), P("z", None), P(), P(), P())
    return jax.shard_map(
        per_device,
        mesh=split,
        in_specs=placed,
        out_specs=(frames, frames, frames, P(None, FRAME_AXES)),
        check_vma=False,
    )
```

```python
import jax
import jax.numpy as jnp
from jax import lax
from jax.sharding import Mesh, PartitionSpec as P

C = 512
TAPS = 7
DILATION_SIZE = 9
FRAME_AXES = ("x", "y", "c", "z")
SCATTER_ORDER = ("c", "z", "y", "x")
EXTRA_COLUMNS = 128


def shift_rows(block, tap_offset, fill):
    rows = block.shape[0]
    shift_amount = min(abs(tap_offset), rows)
    if shift_amount == 0:
        return block
    edge_padding = jnp.full((shift_amount,) + block.shape[1:], fill, block.dtype)
    if tap_offset > 0:
        return jnp.concatenate([block[shift_amount:], edge_padding], axis=0)
    return jnp.concatenate([edge_padding, block[: rows - shift_amount]], axis=0)


def clip_masks(lengths_row, rows):
    clip_ends = jnp.cumsum(lengths_row)
    position = jnp.arange(rows, dtype=jnp.int32)
    clip_id = jnp.sum((position[:, None] >= clip_ends[None, :]).astype(jnp.int32), axis=1)
    result = []
    for kernel_tap_index in range(TAPS):
        tap_offset = (kernel_tap_index - 3) * DILATION_SIZE
        result.append(shift_rows(clip_id, tap_offset, -1) == clip_id)
    return result


def snake_parts(value, alpha):
    sine = jnp.sin(alpha * value)
    double = jnp.sin(2.0 * alpha * value)
    return (
        value + sine * sine / alpha,
        1.0 + double,
        value * double / alpha - sine * sine / (alpha * alpha),
    )


def permute_scatter(value, axis):
    n = lax.axis_size(axis)
    me = lax.axis_index(axis)
    each = value.shape[0] // n
    total = lax.dynamic_slice_in_dim(value, me * each, each)
    for step in range(1, n):
        chunk = lax.dynamic_slice_in_dim(value, ((me + step) % n) * each, each)
        total = total + lax.ppermute(chunk, axis, [(j, (j + step) % n) for j in range(n)])
    return total


def per_device(
    audio, cotangent, clip_lengths, conv_weight, mix_weight, conv_bias, alpha_in, alpha_mid
):
    rows = audio.shape[0]
    same_clip_flags = clip_masks(clip_lengths[0], rows)
    conv_rows = conv_weight.shape[0]
    mix_rows = mix_weight.shape[0]
    both = jnp.concatenate([conv_weight, mix_weight], axis=0)
    gathered = lax.all_gather(both, "z", axis=0, tiled=True)
    gathered = gathered.reshape(-1, conv_rows + mix_rows, C)
    conv_full = gathered[:, :conv_rows].reshape(-1, C)
    mix_full = gathered[:, conv_rows:].reshape(-1, C)
    audio_f = audio.astype(jnp.float32)
    act_in, slope_in, dalpha_in = snake_parts(audio_f, alpha_in)
    first = act_in.astype(jnp.bfloat16)
    columns = []
    for kernel_tap_index in range(TAPS):
        tap_offset = (kernel_tap_index - 3) * DILATION_SIZE
        moved = shift_rows(first, tap_offset, 0)
        columns.append(
            jnp.where(same_clip_flags[kernel_tap_index][:, None], moved, jnp.zeros_like(moved))
        )
    unfolded = jnp.concatenate(columns, axis=1)
    product = jnp.dot(
        unfolded,
        conv_full,
        preferred_element_type=jnp.float32,
    )
    pre = product + conv_bias
    act_mid, slope_mid, dalpha_mid = snake_parts(pre, alpha_mid)
    second = act_mid.astype(jnp.bfloat16)
    second_gradient = lax.dot_general(
        cotangent, mix_full, (((1,), (1,)), ((), ())), preferred_element_type=jnp.float32
    )
    d_pre = (second_gradient * slope_mid).astype(jnp.bfloat16)
    d_unf = lax.dot_general(
        d_pre,
        conv_full,
        (((1,), (1,)), ((), ())),
        preferred_element_type=jnp.float32,
    ).astype(jnp.bfloat16)
    d_first = jnp.zeros((rows, C), jnp.float32)
    for kernel_tap_index in range(TAPS):
        tap_offset = (kernel_tap_index - 3) * DILATION_SIZE
        piece = d_unf[:, kernel_tap_index * C : (kernel_tap_index + 1) * C].astype(jnp.float32)
        piece = jnp.where(same_clip_flags[kernel_tap_index][:, None], piece, jnp.zeros_like(piece))
        d_first = d_first + shift_rows(piece, -tap_offset, 0.0)
    in_grad = (cotangent.astype(jnp.float32) + d_first * slope_in).astype(jnp.bfloat16)
    vectors = jnp.stack(
        [
            jnp.sum(d_pre.astype(jnp.float32), axis=0),
            jnp.sum(cotangent.astype(jnp.float32), axis=0),
            jnp.sum(d_first * dalpha_in, axis=0),
            jnp.sum(second_gradient * dalpha_mid, axis=0),
        ]
    )
    sizes = [lax.axis_size(a) for a in FRAME_AXES]
    devices = 1
    for s in sizes:
        devices *= s
    conv_each = unfolded.shape[1] // devices
    mix_each = second.shape[1] // devices
    order = [FRAME_AXES.index(a) for a in SCATTER_ORDER]

    def lay_out(left):
        left = jnp.concatenate(left, axis=2).reshape(rows, *sizes, conv_each + mix_each)
        return left.transpose(0, *[o + 1 for o in order], 5).reshape(rows, -1)

    conv_lhs = lay_out([unfolded.reshape(rows, devices, conv_each), jnp.zeros((rows, devices, mix_each), unfolded.dtype)])
    mix_lhs = lay_out([jnp.zeros((rows, devices, conv_each), second.dtype), second.reshape(rows, devices, mix_each)])
    packed = lax.dot_general(
        jnp.concatenate([conv_lhs, mix_lhs], axis=0),
        jnp.concatenate([d_pre, cotangent], axis=0),
        (((0,), (0,)), ((), ())),
        preferred_element_type=jnp.float32,
    )
    first_axis, second_axis, *rest = SCATTER_ORDER
    packed = lax.psum_scatter(packed, first_axis, scatter_dimension=0, tiled=True)
    vectors = lax.psum(vectors, first_axis)
    packed, vectors = lax.optimization_barrier((packed, vectors))
    packed = lax.psum_scatter(packed.astype(jnp.bfloat16), second_axis, scatter_dimension=0, tiled=True)
    packed = packed.astype(jnp.float32)
    vectors = lax.psum(vectors, second_axis)
    block = conv_each + mix_each
    held = packed.shape[0] // block
    share = vectors.shape[1] // devices
    vec_blocks = vectors.reshape(4, devices, share).transpose(1, 0, 2).reshape(*sizes, 4 * share)
    kept_names = list(FRAME_AXES)
    for axis in (first_axis, second_axis):
        position = kept_names.index(axis)
        vec_blocks = jnp.take(vec_blocks, lax.axis_index(axis), axis=position)
        kept_names.pop(position)
    vec_blocks = vec_blocks.transpose(*[kept_names.index(a) for a in rest], len(kept_names))
    vec_blocks = vec_blocks.reshape(held, 4 * share)
    extra = jnp.zeros((held, block, EXTRA_COLUMNS), jnp.float32)
    extra = extra.at[:, 0, : 4 * share].set(vec_blocks)
    packed = jnp.concatenate([packed.reshape(held, block, C), extra], axis=2)
    packed = packed.reshape(held * block, C + EXTRA_COLUMNS)
    for axis in rest:
        packed = permute_scatter(packed, axis)
    conv_grad = packed[:conv_each, :C]
    mix_grad = packed[conv_each:, :C]
    vector_grad = packed[0, C : C + 4 * share].reshape(4, share)
    return (in_grad, conv_grad, mix_grad, vector_grad)


def solution(mesh):
    devices = mesh.devices
    xs = len({d.coords[0] for d in devices.flat})
    ys = len({d.coords[1] for d in devices.flat})
    dp, shard = devices.shape
    split = Mesh(devices.reshape(xs, ys, dp // (xs * ys), shard), FRAME_AXES)
    frames = P(FRAME_AXES)
    placed = (frames, frames, frames, P("z", None), P("z", None), P(), P(), P())
    return jax.shard_map(
        per_device,
        mesh=split,
        in_specs=placed,
        out_specs=(frames, frames, frames, P(None, FRAME_AXES)),
        check_vma=False,
    )
```

```python
import jax
import jax.numpy as jnp
from jax import lax
from jax.sharding import Mesh, PartitionSpec as P

C = 512
TAPS = 7
DILATION_SIZE = 9
FRAME_AXES = ("x", "y", "c", "z")
SCATTER_ORDER = ("c", "z", "y", "x")
EXTRA_COLUMNS = 128


def shift_rows(block, tap_offset, fill):
    rows = block.shape[0]
    shift_amount = min(abs(tap_offset), rows)
    if shift_amount == 0:
        return block
    edge_padding = jnp.full((shift_amount,) + block.shape[1:], fill, block.dtype)
    if tap_offset > 0:
        return jnp.concatenate([block[shift_amount:], edge_padding], axis=0)
    return jnp.concatenate([edge_padding, block[: rows - shift_amount]], axis=0)


def clip_masks(lengths_row, rows):
    clip_ends = jnp.cumsum(lengths_row)
    position = jnp.arange(rows, dtype=jnp.int32)
    clip_id = jnp.sum((position[:, None] >= clip_ends[None, :]).astype(jnp.int32), axis=1)
    result = []
    for kernel_tap_index in range(TAPS):
        tap_offset = (kernel_tap_index - 3) * DILATION_SIZE
        result.append(shift_rows(clip_id, tap_offset, -1) == clip_id)
    return result


def snake_parts(value, alpha):
    sine = jnp.sin(alpha * value)
    double = jnp.sin(2.0 * alpha * value)
    return (
        value + sine * sine / alpha,
        1.0 + double,
        value * double / alpha - sine * sine / (alpha * alpha),
    )


def permute_scatter(value, axis):
    n = lax.axis_size(axis)
    me = lax.axis_index(axis)
    each = value.shape[0] // n
    total = lax.dynamic_slice_in_dim(value, me * each, each)
    for step in range(1, n):
        chunk = lax.dynamic_slice_in_dim(value, ((me + step) % n) * each, each)
        total = total + lax.ppermute(chunk, axis, [(j, (j + step) % n) for j in range(n)])
    return total


def per_device(
    audio, cotangent, clip_lengths, conv_weight, mix_weight, conv_bias, alpha_in, alpha_mid
):
    rows = audio.shape[0]
    same_clip_flags = clip_masks(clip_lengths[0], rows)
    conv_rows = conv_weight.shape[0]
    mix_rows = mix_weight.shape[0]
    both = jnp.concatenate([conv_weight, mix_weight], axis=0)
    core = lax.axis_index("c")
    half = C // 2
    own = lax.all_gather(lax.dynamic_slice_in_dim(both, core * half, half, axis=1), "z", axis=0, tiled=True)
    other = lax.ppermute(own, "c", [(0, 1), (1, 0)])
    first_half = jnp.where(core == 0, own, other)
    second_half = jnp.where(core == 0, other, own)
    gathered = jnp.concatenate([first_half, second_half], axis=1)
    gathered = gathered.reshape(-1, conv_rows + mix_rows, C)
    conv_full = gathered[:, :conv_rows].reshape(-1, C)
    mix_full = gathered[:, conv_rows:].reshape(-1, C)
    audio_f = audio.astype(jnp.float32)
    act_in, slope_in, dalpha_in = snake_parts(audio_f, alpha_in)
    first = act_in.astype(jnp.bfloat16)
    columns = []
    for kernel_tap_index in range(TAPS):
        tap_offset = (kernel_tap_index - 3) * DILATION_SIZE
        moved = shift_rows(first, tap_offset, 0)
        columns.append(
            jnp.where(same_clip_flags[kernel_tap_index][:, None], moved, jnp.zeros_like(moved))
        )
    unfolded = jnp.concatenate(columns, axis=1)
    product = jnp.dot(
        unfolded,
        conv_full,
        preferred_element_type=jnp.float32,
    )
    pre = product + conv_bias
    act_mid, slope_mid, dalpha_mid = snake_parts(pre, alpha_mid)
    second = act_mid.astype(jnp.bfloat16)
    second_gradient = lax.dot_general(
        cotangent, mix_full, (((1,), (1,)), ((), ())), preferred_element_type=jnp.float32
    )
    d_pre = (second_gradient * slope_mid).astype(jnp.bfloat16)
    d_unf = lax.dot_general(
        d_pre,
        conv_full,
        (((1,), (1,)), ((), ())),
        preferred_element_type=jnp.float32,
    ).astype(jnp.bfloat16)
    d_first = jnp.zeros((rows, C), jnp.float32)
    for kernel_tap_index in range(TAPS):
        tap_offset = (kernel_tap_index - 3) * DILATION_SIZE
        piece = d_unf[:, kernel_tap_index * C : (kernel_tap_index + 1) * C].astype(jnp.float32)
        piece = jnp.where(same_clip_flags[kernel_tap_index][:, None], piece, jnp.zeros_like(piece))
        d_first = d_first + shift_rows(piece, -tap_offset, 0.0)
    in_grad = (cotangent.astype(jnp.float32) + d_first * slope_in).astype(jnp.bfloat16)
    vectors = jnp.stack(
        [
            jnp.sum(d_pre.astype(jnp.float32), axis=0),
            jnp.sum(cotangent.astype(jnp.float32), axis=0),
            jnp.sum(d_first * dalpha_in, axis=0),
            jnp.sum(second_gradient * dalpha_mid, axis=0),
        ]
    )
    sizes = [lax.axis_size(a) for a in FRAME_AXES]
    devices = 1
    for s in sizes:
        devices *= s
    conv_each = unfolded.shape[1] // devices
    mix_each = second.shape[1] // devices
    order = [FRAME_AXES.index(a) for a in SCATTER_ORDER]

    def lay_out(left):
        left = jnp.concatenate(left, axis=2).reshape(rows, *sizes, conv_each + mix_each)
        return left.transpose(0, *[o + 1 for o in order], 5).reshape(rows, -1)

    conv_lhs = lay_out([unfolded.reshape(rows, devices, conv_each), jnp.zeros((rows, devices, mix_each), unfolded.dtype)])
    mix_lhs = lay_out([jnp.zeros((rows, devices, conv_each), second.dtype), second.reshape(rows, devices, mix_each)])
    packed = lax.dot_general(
        jnp.concatenate([conv_lhs, mix_lhs], axis=0),
        jnp.concatenate([d_pre, cotangent], axis=0),
        (((0,), (0,)), ((), ())),
        preferred_element_type=jnp.float32,
    )
    first_axis, second_axis, *rest = SCATTER_ORDER
    packed = lax.psum_scatter(packed, first_axis, scatter_dimension=0, tiled=True)
    vectors = lax.psum(vectors, first_axis)
    packed, vectors = lax.optimization_barrier((packed, vectors))
    packed = lax.psum_scatter(packed.astype(jnp.bfloat16), second_axis, scatter_dimension=0, tiled=True)
    packed = packed.astype(jnp.float32)
    vectors = lax.psum(vectors, second_axis)
    block = conv_each + mix_each
    held = packed.shape[0] // block
    share = vectors.shape[1] // devices
    vec_blocks = vectors.reshape(4, devices, share).transpose(1, 0, 2).reshape(*sizes, 4 * share)
    kept_names = list(FRAME_AXES)
    for axis in (first_axis, second_axis):
        position = kept_names.index(axis)
        vec_blocks = jnp.take(vec_blocks, lax.axis_index(axis), axis=position)
        kept_names.pop(position)
    vec_blocks = vec_blocks.transpose(*[kept_names.index(a) for a in rest], len(kept_names))
    vec_blocks = vec_blocks.reshape(held, 4 * share)
    extra = jnp.zeros((held, block, EXTRA_COLUMNS), jnp.float32)
    extra = extra.at[:, 0, : 4 * share].set(vec_blocks)
    packed = jnp.concatenate([packed.reshape(held, block, C), extra], axis=2)
    packed = packed.reshape(held * block, C + EXTRA_COLUMNS)
    for axis in rest:
        packed = permute_scatter(packed, axis)
    conv_grad = packed[:conv_each, :C]
    mix_grad = packed[conv_each:, :C]
    vector_grad = packed[0, C : C + 4 * share].reshape(4, share)
    return (in_grad, conv_grad, mix_grad, vector_grad)


def solution(mesh):
    devices = mesh.devices
    xs = len({d.coords[0] for d in devices.flat})
    ys = len({d.coords[1] for d in devices.flat})
    dp, shard = devices.shape
    split = Mesh(devices.reshape(xs, ys, dp // (xs * ys), shard), FRAME_AXES)
    frames = P(FRAME_AXES)
    placed = (frames, frames, frames, P("z", None), P("z", None), P(), P(), P())
    return jax.shard_map(
        per_device,
        mesh=split,
        in_specs=placed,
        out_specs=(frames, frames, frames, P(None, FRAME_AXES)),
        check_vma=False,
    )
```

```python
import jax
import jax.numpy as jnp
from jax import lax
from jax.sharding import Mesh, PartitionSpec as P

C = 512
TAPS = 7
DILATION_SIZE = 9
FRAME_AXES = ("x", "y", "c", "z")
SCATTER_ORDER = ("c", "z", "y", "x")
EXTRA_COLUMNS = 128


def shift_rows(block, tap_offset, fill):
    rows = block.shape[0]
    shift_amount = min(abs(tap_offset), rows)
    if shift_amount == 0:
        return block
    edge_padding = jnp.full((shift_amount,) + block.shape[1:], fill, block.dtype)
    if tap_offset > 0:
        return jnp.concatenate([block[shift_amount:], edge_padding], axis=0)
    return jnp.concatenate([edge_padding, block[: rows - shift_amount]], axis=0)


def clip_masks(lengths_row, rows):
    clip_ends = jnp.cumsum(lengths_row)
    position = jnp.arange(rows, dtype=jnp.int32)
    clip_id = jnp.sum((position[:, None] >= clip_ends[None, :]).astype(jnp.int32), axis=1)
    result = []
    for kernel_tap_index in range(TAPS):
        tap_offset = (kernel_tap_index - 3) * DILATION_SIZE
        result.append(shift_rows(clip_id, tap_offset, -1) == clip_id)
    return result


def snake_parts(value, alpha):
    sine = jnp.sin(alpha * value)
    double = jnp.sin(2.0 * alpha * value)
    return (
        value + sine * sine / alpha,
        1.0 + double,
        value * double / alpha - sine * sine / (alpha * alpha),
    )


def permute_scatter(value, axis):
    n = lax.axis_size(axis)
    me = lax.axis_index(axis)
    each = value.shape[0] // n
    total = lax.dynamic_slice_in_dim(value, me * each, each)
    for step in range(1, n):
        chunk = lax.dynamic_slice_in_dim(value, ((me + step) % n) * each, each)
        total = total + lax.ppermute(chunk, axis, [(j, (j + step) % n) for j in range(n)])
    return total


def per_device(
    audio, cotangent, clip_lengths, conv_weight, mix_weight, conv_bias, alpha_in, alpha_mid
):
    rows = audio.shape[0]
    same_clip_flags = clip_masks(clip_lengths[0], rows)
    conv_rows = conv_weight.shape[0]
    mix_rows = mix_weight.shape[0]
    both = jnp.concatenate([conv_weight, mix_weight], axis=0)
    core = lax.axis_index("c")
    half = C // 2
    own = lax.all_gather(lax.dynamic_slice_in_dim(both, core * half, half, axis=1), "z", axis=0, tiled=True)
    audio_f = audio.astype(jnp.float32)
    act_in, slope_in, dalpha_in = snake_parts(audio_f, alpha_in)
    first = act_in.astype(jnp.bfloat16)
    columns = []
    for kernel_tap_index in range(TAPS):
        tap_offset = (kernel_tap_index - 3) * DILATION_SIZE
        moved = shift_rows(first, tap_offset, 0)
        columns.append(
            jnp.where(same_clip_flags[kernel_tap_index][:, None], moved, jnp.zeros_like(moved))
        )
    unfolded = jnp.concatenate(columns, axis=1)
    sizes = [lax.axis_size(a) for a in FRAME_AXES]
    devices = 1
    for s in sizes:
        devices *= s
    conv_each = unfolded.shape[1] // devices
    mix_each = C // devices
    order = [FRAME_AXES.index(a) for a in SCATTER_ORDER]

    def lay_out(left):
        left = jnp.concatenate(left, axis=2).reshape(rows, *sizes, conv_each + mix_each)
        return left.transpose(0, *[o + 1 for o in order], 5).reshape(rows, -1)

    conv_lhs = lay_out([unfolded.reshape(rows, devices, conv_each), jnp.zeros((rows, devices, mix_each), unfolded.dtype)])
    own, conv_lhs = lax.optimization_barrier((own, conv_lhs))
    other = lax.ppermute(own, "c", [(0, 1), (1, 0)])
    first_half = jnp.where(core == 0, own, other)
    second_half = jnp.where(core == 0, other, own)
    gathered = jnp.concatenate([first_half, second_half], axis=1)
    gathered = gathered.reshape(-1, conv_rows + mix_rows, C)
    conv_full = gathered[:, :conv_rows].reshape(-1, C)
    mix_full = gathered[:, conv_rows:].reshape(-1, C)
    product = jnp.dot(
        unfolded,
        conv_full,
        preferred_element_type=jnp.float32,
    )
    pre = product + conv_bias
    act_mid, slope_mid, dalpha_mid = snake_parts(pre, alpha_mid)
    second = act_mid.astype(jnp.bfloat16)
    second_gradient = lax.dot_general(
        cotangent, mix_full, (((1,), (1,)), ((), ())), preferred_element_type=jnp.float32
    )
    d_pre = (second_gradient * slope_mid).astype(jnp.bfloat16)
    d_unf = lax.dot_general(
        d_pre,
        conv_full,
        (((1,), (1,)), ((), ())),
        preferred_element_type=jnp.float32,
    ).astype(jnp.bfloat16)
    d_first = jnp.zeros((rows, C), jnp.float32)
    for kernel_tap_index in range(TAPS):
        tap_offset = (kernel_tap_index - 3) * DILATION_SIZE
        piece = d_unf[:, kernel_tap_index * C : (kernel_tap_index + 1) * C].astype(jnp.float32)
        piece = jnp.where(same_clip_flags[kernel_tap_index][:, None], piece, jnp.zeros_like(piece))
        d_first = d_first + shift_rows(piece, -tap_offset, 0.0)
    in_grad = (cotangent.astype(jnp.float32) + d_first * slope_in).astype(jnp.bfloat16)
    vectors = jnp.stack(
        [
            jnp.sum(d_pre.astype(jnp.float32), axis=0),
            jnp.sum(cotangent.astype(jnp.float32), axis=0),
            jnp.sum(d_first * dalpha_in, axis=0),
            jnp.sum(second_gradient * dalpha_mid, axis=0),
        ]
    )
    mix_lhs = lay_out([jnp.zeros((rows, devices, conv_each), second.dtype), second.reshape(rows, devices, mix_each)])
    packed = lax.dot_general(
        jnp.concatenate([conv_lhs, mix_lhs], axis=0),
        jnp.concatenate([d_pre, cotangent], axis=0),
        (((0,), (0,)), ((), ())),
        preferred_element_type=jnp.float32,
    )
    first_axis, second_axis, *rest = SCATTER_ORDER
    packed = lax.psum_scatter(packed, first_axis, scatter_dimension=0, tiled=True)
    vectors = lax.psum(vectors, first_axis)
    packed, vectors = lax.optimization_barrier((packed, vectors))
    packed = lax.psum_scatter(packed.astype(jnp.bfloat16), second_axis, scatter_dimension=0, tiled=True)
    packed = packed.astype(jnp.float32)
    vectors = lax.psum(vectors, second_axis)
    block = conv_each + mix_each
    held = packed.shape[0] // block
    share = vectors.shape[1] // devices
    vec_blocks = vectors.reshape(4, devices, share).transpose(1, 0, 2).reshape(*sizes, 4 * share)
    kept_names = list(FRAME_AXES)
    for axis in (first_axis, second_axis):
        position = kept_names.index(axis)
        vec_blocks = jnp.take(vec_blocks, lax.axis_index(axis), axis=position)
        kept_names.pop(position)
    vec_blocks = vec_blocks.transpose(*[kept_names.index(a) for a in rest], len(kept_names))
    vec_blocks = vec_blocks.reshape(held, 4 * share)
    extra = jnp.zeros((held, block, EXTRA_COLUMNS), jnp.float32)
    extra = extra.at[:, 0, : 4 * share].set(vec_blocks)
    packed = jnp.concatenate([packed.reshape(held, block, C), extra], axis=2)
    packed = packed.reshape(held * block, C + EXTRA_COLUMNS)
    for axis in rest:
        packed = permute_scatter(packed, axis)
    conv_grad = packed[:conv_each, :C]
    mix_grad = packed[conv_each:, :C]
    vector_grad = packed[0, C : C + 4 * share].reshape(4, share)
    return (in_grad, conv_grad, mix_grad, vector_grad)


def solution(mesh):
    devices = mesh.devices
    xs = len({d.coords[0] for d in devices.flat})
    ys = len({d.coords[1] for d in devices.flat})
    dp, shard = devices.shape
    split = Mesh(devices.reshape(xs, ys, dp // (xs * ys), shard), FRAME_AXES)
    frames = P(FRAME_AXES)
    placed = (frames, frames, frames, P("z", None), P("z", None), P(), P(), P())
    return jax.shard_map(
        per_device,
        mesh=split,
        in_specs=placed,
        out_specs=(frames, frames, frames, P(None, FRAME_AXES)),
        check_vma=False,
    )
```

```python
import jax
import jax.numpy as jnp
from jax import lax
from jax.sharding import Mesh, PartitionSpec as P

C = 512
TAPS = 7
DILATION_SIZE = 9
FRAME_AXES = ("x", "y", "c", "z")
SCATTER_ORDER = ("c", "z", "y", "x")
EXTRA_COLUMNS = 128


def shift_rows(block, tap_offset, fill):
    rows = block.shape[0]
    shift_amount = min(abs(tap_offset), rows)
    if shift_amount == 0:
        return block
    edge_padding = jnp.full((shift_amount,) + block.shape[1:], fill, block.dtype)
    if tap_offset > 0:
        return jnp.concatenate([block[shift_amount:], edge_padding], axis=0)
    return jnp.concatenate([edge_padding, block[: rows - shift_amount]], axis=0)


def clip_masks(lengths_row, rows):
    clip_ends = jnp.cumsum(lengths_row)
    position = jnp.arange(rows, dtype=jnp.int32)
    clip_id = jnp.sum((position[:, None] >= clip_ends[None, :]).astype(jnp.int32), axis=1)
    result = []
    for kernel_tap_index in range(TAPS):
        tap_offset = (kernel_tap_index - 3) * DILATION_SIZE
        result.append(shift_rows(clip_id, tap_offset, -1) == clip_id)
    return result


def snake_parts(value, alpha):
    sine = jnp.sin(alpha * value)
    double = jnp.sin(2.0 * alpha * value)
    return (
        value + sine * sine / alpha,
        1.0 + double,
        value * double / alpha - sine * sine / (alpha * alpha),
    )


def permute_scatter(value, axis):
    n = lax.axis_size(axis)
    me = lax.axis_index(axis)
    each = value.shape[0] // n
    total = lax.dynamic_slice_in_dim(value, me * each, each)
    for step in range(1, n):
        chunk = lax.dynamic_slice_in_dim(value, ((me + step) % n) * each, each)
        total = total + lax.ppermute(chunk, axis, [(j, (j + step) % n) for j in range(n)])
    return total


def per_device(
    audio, cotangent, clip_lengths, conv_weight, mix_weight, conv_bias, alpha_in, alpha_mid
):
    rows = audio.shape[0]
    same_clip_flags = clip_masks(clip_lengths[0], rows)
    conv_rows = conv_weight.shape[0]
    mix_rows = mix_weight.shape[0]
    both = jnp.concatenate([conv_weight, mix_weight], axis=0)
    core = lax.axis_index("c")
    half = C // 2
    own = lax.all_gather(lax.dynamic_slice_in_dim(both, core * half, half, axis=1), "z", axis=0, tiled=True)
    audio_f = audio.astype(jnp.float32)
    act_in, slope_in, dalpha_in = snake_parts(audio_f, alpha_in)
    first = act_in.astype(jnp.bfloat16)
    columns = []
    for kernel_tap_index in range(TAPS):
        tap_offset = (kernel_tap_index - 3) * DILATION_SIZE
        moved = shift_rows(first, tap_offset, 0)
        columns.append(
            jnp.where(same_clip_flags[kernel_tap_index][:, None], moved, jnp.zeros_like(moved))
        )
    unfolded = jnp.concatenate(columns, axis=1)
    sizes = [lax.axis_size(a) for a in FRAME_AXES]
    devices = 1
    for s in sizes:
        devices *= s
    conv_each = unfolded.shape[1] // devices
    mix_each = C // devices
    order = [FRAME_AXES.index(a) for a in SCATTER_ORDER]

    def lay_out(left):
        left = jnp.concatenate(left, axis=2).reshape(rows, *sizes, conv_each + mix_each)
        return left.transpose(0, *[o + 1 for o in order], 5).reshape(rows, -1)

    conv_lhs = lay_out([unfolded.reshape(rows, devices, conv_each), jnp.zeros((rows, devices, mix_each), unfolded.dtype)])
    own, conv_lhs = lax.optimization_barrier((own, conv_lhs))
    other = lax.ppermute(own, "c", [(0, 1), (1, 0)])
    first_half = jnp.where(core == 0, own, other)
    second_half = jnp.where(core == 0, other, own)
    gathered = jnp.concatenate([first_half, second_half], axis=1)
    gathered = gathered.reshape(-1, conv_rows + mix_rows, C)
    conv_full = gathered[:, :conv_rows].reshape(-1, C)
    mix_full = gathered[:, conv_rows:].reshape(-1, C)
    product = jnp.dot(
        unfolded,
        conv_full,
        preferred_element_type=jnp.float32,
    )
    pre = product + conv_bias
    act_mid, slope_mid, dalpha_mid = snake_parts(pre, alpha_mid)
    second = act_mid.astype(jnp.bfloat16)
    second_gradient = lax.dot_general(
        cotangent, mix_full, (((1,), (1,)), ((), ())), preferred_element_type=jnp.float32
    )
    d_pre = (second_gradient * slope_mid).astype(jnp.bfloat16)
    d_unf = lax.dot_general(
        d_pre,
        conv_full,
        (((1,), (1,)), ((), ())),
        preferred_element_type=jnp.float32,
    ).astype(jnp.bfloat16)
    d_first = jnp.zeros((rows, C), jnp.float32)
    for kernel_tap_index in range(TAPS):
        tap_offset = (kernel_tap_index - 3) * DILATION_SIZE
        piece = d_unf[:, kernel_tap_index * C : (kernel_tap_index + 1) * C].astype(jnp.float32)
        piece = jnp.where(same_clip_flags[kernel_tap_index][:, None], piece, jnp.zeros_like(piece))
        d_first = d_first + shift_rows(piece, -tap_offset, 0.0)
    in_grad = (cotangent.astype(jnp.float32) + d_first * slope_in).astype(jnp.bfloat16)
    vectors = jnp.stack(
        [
            jnp.sum(d_pre.astype(jnp.float32), axis=0),
            jnp.sum(cotangent.astype(jnp.float32), axis=0),
            jnp.sum(d_first * dalpha_in, axis=0),
            jnp.sum(second_gradient * dalpha_mid, axis=0),
        ]
    )
    mix_lhs = lay_out([jnp.zeros((rows, devices, conv_each), second.dtype), second.reshape(rows, devices, mix_each)])
    packed = lax.dot_general(
        jnp.concatenate([conv_lhs, mix_lhs], axis=0),
        jnp.concatenate([d_pre, cotangent], axis=0),
        (((0,), (0,)), ((), ())),
        preferred_element_type=jnp.float32,
    )
    first_axis, second_axis, *rest = SCATTER_ORDER
    packed = lax.psum_scatter(packed.astype(jnp.bfloat16), first_axis, scatter_dimension=0, tiled=True)
    vectors = lax.psum(vectors, first_axis)
    packed, vectors = lax.optimization_barrier((packed, vectors))
    packed = lax.psum_scatter(packed, second_axis, scatter_dimension=0, tiled=True)
    packed = packed.astype(jnp.float32)
    vectors = lax.psum(vectors, second_axis)
    block = conv_each + mix_each
    held = packed.shape[0] // block
    share = vectors.shape[1] // devices
    vec_blocks = vectors.reshape(4, devices, share).transpose(1, 0, 2).reshape(*sizes, 4 * share)
    kept_names = list(FRAME_AXES)
    for axis in (first_axis, second_axis):
        position = kept_names.index(axis)
        vec_blocks = jnp.take(vec_blocks, lax.axis_index(axis), axis=position)
        kept_names.pop(position)
    vec_blocks = vec_blocks.transpose(*[kept_names.index(a) for a in rest], len(kept_names))
    vec_blocks = vec_blocks.reshape(held, 4 * share)
    extra = jnp.zeros((held, block, EXTRA_COLUMNS), jnp.float32)
    extra = extra.at[:, 0, : 4 * share].set(vec_blocks)
    packed = jnp.concatenate([packed.reshape(held, block, C), extra], axis=2)
    packed = packed.reshape(held * block, C + EXTRA_COLUMNS)
    for axis in rest:
        packed = permute_scatter(packed, axis)
    conv_grad = packed[:conv_each, :C]
    mix_grad = packed[conv_each:, :C]
    vector_grad = packed[0, C : C + 4 * share].reshape(4, share)
    return (in_grad, conv_grad, mix_grad, vector_grad)


def solution(mesh):
    devices = mesh.devices
    xs = len({d.coords[0] for d in devices.flat})
    ys = len({d.coords[1] for d in devices.flat})
    dp, shard = devices.shape
    split = Mesh(devices.reshape(xs, ys, dp // (xs * ys), shard), FRAME_AXES)
    frames = P(FRAME_AXES)
    placed = (frames, frames, frames, P("z", None), P("z", None), P(), P(), P())
    return jax.shard_map(
        per_device,
        mesh=split,
        in_specs=placed,
        out_specs=(frames, frames, frames, P(None, FRAME_AXES)),
        check_vma=False,
    )
```
